512 devices in a mesh: ctx: 64 (over z, y_hi, core), head: 8 (over y_lo, x).
Axes of the slice: x: 4, y: 4 (y_hi: 2, y_lo: 2; y = y_hi * 2 + y_lo), z: 16, core: 2. Of those that a mesh axis runs over, the one named last changes fastest.
Arguments:
- query_states: bfloat16 [32768, 8192], P('ctx', 'head'), may hold values from -5 to 5
- key_states: bfloat16 [32768, 1024], P('ctx', 'head'), may hold values from -5 to 5
- value_states: bfloat16 [32768, 1024], P('ctx', 'head'), may hold values from -6 to 6
- out_grad: bfloat16 [32768, 8192], P('ctx', 'head'), may hold values from -6 to 6
- block_lists: int32 [256, 4], replicated, may hold values from 0 to 255, as said below
Outputs:
- query_grad: bfloat16 [32768, 8192], P(('ctx', 'head'))
- key_grad: bfloat16 [32768, 1024], P(('ctx', 'head'))
- value_grad: bfloat16 [32768, 1024], P(('ctx', 'head'))
The draws below stay inside these ranges and needn't reach their ends.
Inputs may be any that keep to these rules, and one draw needn't show every extreme that they name: `block_lists`: entry 0 of row b is b. The other entries name distinct blocks below b, each held by the same index of ctx as b or by one of the 8 indices just below it; a row with fewer candidates repeats b in its remaining entries. Taken over the 4 rows of one index of ctx, the listed blocks that another index of ctx holds are at most one distinct block.
All inputs are finite; a program needn't handle non-finite values.
Results may differ from the reference program's by a relative error of at most 0.012.
Values may be sent and summed in bfloat16 or wider, within the bound.
No kernel may reach another device: no remote copies, remote signals or barrier semaphores. Data moves between devices by JAX's collectives and lax.ppermute only.
A program may use at most 64 MiB of HBM per device.

```python
import math
import jax
import jax.numpy as jnp
from jax import lax

HEADS = 64
KV_HEADS = 8
HEAD_DIM = 128
BLOCK = 128
TOPK = 3
REACH = 8
SEL = 4
TOKENS = 32768
NB = 256
BDEV = 4


def draw_query_states(key, part):
    base_vals = jnp.clip(jax.random.normal(jax.random.fold_in(key, 1), (TOKENS, HEADS * HEAD_DIM), jnp.float32), -4.8, 4.8)
    return base_vals.astype(jnp.bfloat16)


def draw_key_states(key, part):
    base_vals = jnp.clip(jax.random.normal(jax.random.fold_in(key, 2), (TOKENS, KV_HEADS * HEAD_DIM), jnp.float32), -4.8, 4.8)
    return base_vals.astype(jnp.bfloat16)


def draw_block_lists(key, part):
    dev_count = NB // BDEV
    row_ids = jnp.arange(NB, dtype=jnp.int32)
    col_ids = jnp.arange(NB, dtype=jnp.int32)
    offer_pick = jax.random.randint(jax.random.fold_in(key, 11), (dev_count, dev_count), 0, BDEV, dtype=jnp.int32)
    dev_rows = row_ids // BDEV
    dev_cols = col_ids // BDEV
    offered = offer_pick[dev_rows][:, dev_cols]
    behind = dev_rows[:, None] - dev_cols[None, :]
    remote_ok = (behind >= 1) & (behind <= REACH) & ((col_ids % BDEV)[None, :] == offered)
    local_ok = (behind == 0) & (col_ids[None, :] < row_ids[:, None])
    eligible = remote_ok | local_ok
    scores = jax.random.randint(jax.random.fold_in(key, 12), (NB, NB), 0, 4096, dtype=jnp.int32)
    keyed = jnp.where(eligible, scores * NB + col_ids[None, :], 4096 * NB + col_ids[None, :])
    ranking = jnp.argsort(keyed, axis=1)[:, :TOPK].astype(jnp.int32)
    picked_ok = jnp.take_along_axis(eligible, ranking, axis=1)
    chosen_ids = jnp.where(picked_ok, ranking, row_ids[:, None])
    return jnp.concatenate([row_ids[:, None], chosen_ids], axis=1).astype(jnp.int32)


def block_scale(key, extent, split, low, largest):
    gain = 1.0
    for dim, blocks in split:
        steps = jax.random.uniform(jax.random.fold_in(jax.random.fold_in(key, 6), dim), (blocks,), jnp.float32, low / len(split), largest / len(split))
        gain = gain * jnp.repeat(jnp.exp(steps), extent[dim] // blocks).reshape((-1,) + (1,) * (len(extent) - 1 - dim))
    return gain


def normal_values(rng, extent, spread, reach, pieces=(), kind=jnp.bfloat16):
    drawn = spread * jax.random.normal(rng, extent, jnp.float32)
    if pieces:
        drawn = drawn * block_scale(rng, extent, pieces, -0.22, 0.18)
    return jnp.clip(drawn, -reach, reach).astype(kind)


def setup_inputs(seed: int = 0) -> dict:
    key_of = jax.random.split(jax.random.key(seed), 6)
    query_states = draw_query_states(jax.random.fold_in(key_of[5], 71), 0)
    key_states = draw_key_states(jax.random.fold_in(key_of[5], 71), 0)
    value_states = normal_values(key_of[2], (TOKENS, KV_HEADS * HEAD_DIM), 1.0, 6.0, ((0, 64), (1, 8)))
    out_grad = normal_values(key_of[3], (TOKENS, HEADS * HEAD_DIM), 1.0, 6.0, ((0, 64), (1, 8)))
    block_lists = draw_block_lists(jax.random.fold_in(key_of[5], 71), 0)
    return dict(query_states=query_states, key_states=key_states, value_states=value_states, out_grad=out_grad, block_lists=block_lists)


def reference(query_states, key_states, value_states, out_grad, block_lists):
    group_size = HEADS // KV_HEADS
    scaling = 1.0 / math.sqrt(HEAD_DIM)
    query_all = query_states.reshape(NB, BLOCK, KV_HEADS, group_size, HEAD_DIM)
    grad_all = out_grad.reshape(NB, BLOCK, KV_HEADS, group_size, HEAD_DIM)
    key_all = key_states.reshape(NB, BLOCK, KV_HEADS, HEAD_DIM)
    value_all = value_states.reshape(NB, BLOCK, KV_HEADS, HEAD_DIM)
    positions = jnp.arange(BLOCK, dtype=jnp.int32)
    causal = positions[None, :] <= positions[:, None]
    order_ids = jnp.arange(SEL, dtype=jnp.int32)

    def one_block(running, block_id):
        key_acc, value_acc = running
        entries = block_lists[block_id]
        query_blk = query_all[block_id].astype(jnp.float32)
        grad_blk = grad_all[block_id].astype(jnp.float32)
        key_blk = key_all[entries].astype(jnp.float32)
        value_blk = value_all[entries].astype(jnp.float32)
        repeat = (entries[:, None] == entries[None, :]) & (order_ids[None, :] < order_ids[:, None])
        usable = jnp.logical_not(jnp.any(repeat, axis=1))
        allowed = usable[None, :, None] & ((entries < block_id)[None, :, None] | causal[:, None, :])
        scores = jnp.einsum('ighd,etgd->ghiet', query_blk, key_blk) * scaling
        scores = jnp.where(allowed, scores, -1e+30)
        row_max = lax.optimization_barrier(jnp.max(scores, axis=(3, 4), keepdims=True))
        total = lax.optimization_barrier(jnp.sum(jnp.where(allowed, jnp.exp(scores - row_max), 0.0), axis=(3, 4), keepdims=True))
        log_total = row_max + jnp.log(total)
        prob = jnp.where(allowed, jnp.exp(scores - log_total), 0.0)
        prob_half = lax.optimization_barrier(prob.astype(jnp.bfloat16)).astype(jnp.float32)
        output = jnp.einsum('ghiet,etgd->ighd', prob_half, value_blk).astype(jnp.bfloat16)
        output_wide = lax.optimization_barrier(output).astype(jnp.float32)
        row_dot = lax.optimization_barrier(jnp.sum(grad_blk * output_wide, axis=-1))
        prob_grad = jnp.einsum('ighd,etgd->ghiet', grad_blk, value_blk)
        centred = prob_grad - jnp.transpose(row_dot, (1, 2, 0))[..., None, None]
        score_grad = (prob * centred * scaling).astype(jnp.bfloat16)
        score_wide = lax.optimization_barrier(score_grad).astype(jnp.float32)
        block_qgrad = jnp.einsum('ghiet,etgd->ighd', score_wide, key_blk).astype(jnp.bfloat16)
        key_part = jnp.einsum('ghiet,ighd->etgd', score_wide, query_blk)
        value_part = jnp.einsum('ghiet,ighd->etgd', prob_half, grad_blk)
        key_acc = key_acc.at[entries].add(key_part)
        value_acc = value_acc.at[entries].add(value_part)
        return ((key_acc, value_acc), block_qgrad)
    zeros_acc = jnp.zeros((NB, BLOCK, KV_HEADS, HEAD_DIM), jnp.float32)
    (key_acc, value_acc), query_parts = lax.scan(one_block, (zeros_acc, zeros_acc), jnp.arange(NB, dtype=jnp.int32))
    query_grad = query_parts.reshape(TOKENS, HEADS * HEAD_DIM)
    key_grad = key_acc.reshape(TOKENS, KV_HEADS * HEAD_DIM).astype(jnp.bfloat16)
    value_grad = value_acc.reshape(TOKENS, KV_HEADS * HEAD_DIM).astype(jnp.bfloat16)
    return (query_grad, key_grad, value_grad)
```

```python
import functools
import math

import jax
import jax.numpy as jnp
from jax import lax
from jax.experimental import pallas as pl
from jax.experimental.pallas import tpu as pltpu
from jax.sharding import PartitionSpec as P

HEADS = 64
KV_HEADS = 8
HEAD_DIM = 128
BLOCK = 128
REACH = 8


def from_behind(x, axis, by):
    devices = lax.axis_size(axis)
    pairs = [(i, i + by) for i in range(devices) if 0 <= i + by < devices]
    return lax.ppermute(x, axis, pairs)


def attn_kernel(slot_ref, use_ref, early_ref, q_ref, g_ref, kv_ref, dq_ref, acc_ref, kv_scr, dk_scr, dv_scr,
                *, chosen, group, scaling):
    n = pl.program_id(0)

    @pl.when(n == 0)
    def _():
        acc_ref[...] = jnp.zeros_like(acc_ref)

    keys = chosen * BLOCK
    for e in range(chosen):
        kv_scr[e * BLOCK:(e + 1) * BLOCK, :] = kv_ref[slot_ref[n * chosen + e]]
    key_cat = kv_scr[:, :HEAD_DIM]
    value_cat = kv_scr[:, HEAD_DIM:]

    col = lax.broadcasted_iota(jnp.int32, (BLOCK, keys), 1)
    row = lax.broadcasted_iota(jnp.int32, (BLOCK, keys), 0)
    ent = col // BLOCK
    tok = col % BLOCK
    use_col = jnp.zeros((BLOCK, keys), jnp.int32)
    early_col = jnp.zeros((BLOCK, keys), jnp.int32)
    for e in range(chosen):
        use_col = jnp.where(ent == e, use_ref[n * chosen + e], use_col)
        early_col = jnp.where(ent == e, early_ref[n * chosen + e], early_col)
    allowed = (use_col != 0) & ((early_col != 0) | (tok <= row))

    dk_scr[...] = jnp.zeros_like(dk_scr)
    dv_scr[...] = jnp.zeros_like(dv_scr)
    nt = (((1,), (1,)), ((), ()))
    tn = (((0,), (0,)), ((), ()))
    for h in range(group):
        cols = slice(h * HEAD_DIM, (h + 1) * HEAD_DIM)
        q_h = q_ref[:, cols]
        g_h = g_ref[:, cols]
        scores = lax.dot_general(q_h, key_cat, nt, preferred_element_type=jnp.float32) * scaling
        scores = jnp.where(allowed, scores, -1e30)
        row_max = jnp.max(scores, axis=1, keepdims=True)
        total = jnp.sum(jnp.where(allowed, jnp.exp(scores - row_max), 0.0), axis=1, keepdims=True)
        log_total = row_max + jnp.log(total)
        prob = jnp.where(allowed, jnp.exp(scores - log_total), 0.0)
        prob_half = prob.astype(jnp.bfloat16)
        output = jnp.dot(prob_half, value_cat, preferred_element_type=jnp.float32)
        output = output.astype(jnp.bfloat16).astype(jnp.float32)
        row_dot = jnp.sum(g_h.astype(jnp.float32) * output, axis=1, keepdims=True)
        prob_grad = lax.dot_general(g_h, value_cat, nt, preferred_element_type=jnp.float32)
        score_grad = (prob * (prob_grad - row_dot) * scaling).astype(jnp.bfloat16)
        dq_h = jnp.dot(score_grad, key_cat, preferred_element_type=jnp.float32)
        dq_ref[:, cols] = dq_h.astype(jnp.bfloat16)
        dk_scr[...] += lax.dot_general(score_grad, q_h, tn, preferred_element_type=jnp.float32)
        dv_scr[...] += lax.dot_general(prob_half, g_h, tn, preferred_element_type=jnp.float32)

    for e in range(chosen):
        s = slot_ref[n * chosen + e]
        rows = slice(e * BLOCK, (e + 1) * BLOCK)
        acc_ref[s, :, :HEAD_DIM] += dk_scr[rows, :]
        acc_ref[s, :, HEAD_DIM:] += dv_scr[rows, :]


def attention_terms(slots, usable, earlier, query_states, out_grad, kv_stock, chosen):
    tok_rows, q_cols = query_states.shape
    slot_count = kv_stock.shape[0]
    group = q_cols // HEAD_DIM
    blocks_here = tok_rows // BLOCK
    kernel = functools.partial(attn_kernel, chosen=chosen, group=group, scaling=1.0 / math.sqrt(HEAD_DIM))
    grid_spec = pltpu.PrefetchScalarGridSpec(
        num_scalar_prefetch=3,
        grid=(blocks_here,),
        in_specs=[
            pl.BlockSpec((BLOCK, q_cols), lambda n, *_: (n, 0)),
            pl.BlockSpec((BLOCK, q_cols), lambda n, *_: (n, 0)),
            pl.BlockSpec((slot_count, BLOCK, 2 * HEAD_DIM), lambda n, *_: (0, 0, 0)),
        ],
        out_specs=[
            pl.BlockSpec((BLOCK, q_cols), lambda n, *_: (n, 0)),
            pl.BlockSpec((slot_count, BLOCK, 2 * HEAD_DIM), lambda n, *_: (0, 0, 0)),
        ],
        scratch_shapes=[
            pltpu.VMEM((chosen * BLOCK, 2 * HEAD_DIM), jnp.bfloat16),
            pltpu.VMEM((chosen * BLOCK, HEAD_DIM), jnp.float32),
            pltpu.VMEM((chosen * BLOCK, HEAD_DIM), jnp.float32),
        ],
    )
    return pl.pallas_call(
        kernel,
        grid_spec=grid_spec,
        out_shape=[
            jax.ShapeDtypeStruct((tok_rows, q_cols), jnp.bfloat16),
            jax.ShapeDtypeStruct((slot_count, BLOCK, 2 * HEAD_DIM), jnp.float32),
        ],
        compiler_params=pltpu.CompilerParams(dimension_semantics=("arbitrary",)),
    )(slots, usable, earlier, query_states, out_grad, kv_stock)


def body(query_states, key_states, value_states, out_grad, block_lists):
    ctx_count = lax.axis_size("ctx")
    head_count = lax.axis_size("head")
    myself = lax.axis_index("ctx")
    tok_rows = query_states.shape[0]
    kv_cols = key_states.shape[1]
    blocks_here = tok_rows // BLOCK
    chosen = block_lists.shape[1]
    lists_by_dev = block_lists.reshape(ctx_count, blocks_here * chosen)
    slot_ids = jnp.arange(blocks_here, dtype=jnp.int32)
    distances = jnp.arange(1, REACH + 1, dtype=jnp.int32)
    targets = myself + distances
    target_ok = targets < ctx_count
    target_rows = jnp.take(lists_by_dev, jnp.minimum(targets, ctx_count - 1), axis=0)
    mine = target_rows // blocks_here == myself
    requested = jnp.max(jnp.where(mine, target_rows % blocks_here, -1), axis=1)
    requested = jnp.where(target_ok, requested, -1)
    kv_local = jnp.concatenate([key_states, value_states], axis=1).reshape(blocks_here, BLOCK, 2 * kv_cols)
    outgoing = jnp.take(kv_local, jnp.clip(requested, 0, blocks_here - 1), axis=0)
    arrivals = [from_behind(outgoing[d - 1], "ctx", d) for d in range(1, REACH + 1)]
    kv_stock = jnp.concatenate([kv_local, jnp.stack(arrivals, axis=0)], axis=0)

    own_entries = lax.dynamic_slice_in_dim(block_lists, myself * blocks_here, blocks_here, 0)
    block_ids = myself * blocks_here + slot_ids
    order_ids = jnp.arange(chosen, dtype=jnp.int32)
    repeat = (own_entries[:, :, None] == own_entries[:, None, :]) & (
        order_ids[None, None, :] < order_ids[None, :, None]
    )
    usable = jnp.logical_not(jnp.any(repeat, axis=2))
    earlier = own_entries < block_ids[:, None]
    behind = myself - own_entries // blocks_here
    slots = jnp.where(behind == 0, own_entries % blocks_here, blocks_here - 1 + behind)
    slots = jnp.clip(slots, 0, blocks_here + REACH - 1)

    query_local, acc = attention_terms(
        slots.reshape(-1).astype(jnp.int32),
        usable.reshape(-1).astype(jnp.int32),
        earlier.reshape(-1).astype(jnp.int32),
        query_states,
        out_grad,
        kv_stock,
        chosen,
    )
    query_grad = lax.all_to_all(query_local, "head", split_axis=0, concat_axis=1, tiled=True)

    sendback = acc[blocks_here:].astype(jnp.bfloat16)
    returned = [from_behind(sendback[d - 1], "ctx", -d) for d in range(1, REACH + 1)]
    arrived = jnp.stack(returned, axis=0).astype(jnp.float32)
    credit = (requested[None, :] == slot_ids[:, None]).astype(jnp.float32)
    totals = acc[:blocks_here] + jnp.sum(credit[:, :, None, None] * arrived[None], axis=1)
    kv_grad = totals.reshape(tok_rows, 2 * kv_cols).astype(jnp.bfloat16)
    kv_all = lax.all_to_all(kv_grad, "head", split_axis=0, concat_axis=1, tiled=True)
    kv_all = kv_all.reshape(tok_rows // head_count, head_count, 2, kv_cols)
    key_grad = kv_all[:, :, 0, :].reshape(tok_rows // head_count, head_count * kv_cols)
    value_grad = kv_all[:, :, 1, :].reshape(tok_rows // head_count, head_count * kv_cols)
    return (query_grad, key_grad, value_grad)


def solution(mesh):
    in_specs = (P("ctx", "head"), P("ctx", "head"), P("ctx", "head"), P("ctx", "head"), P())
    out_specs = (P(("ctx", "head"), None), P(("ctx", "head"), None), P(("ctx", "head"), None))
    return jax.shard_map(body, mesh=mesh, in_specs=in_specs, out_specs=out_specs, check_vma=False)
```

```python
import functools
import math

import jax
import jax.numpy as jnp
from jax import lax
from jax.experimental import pallas as pl
from jax.experimental.pallas import tpu as pltpu
from jax.sharding import PartitionSpec as P

HEADS = 64
KV_HEADS = 8
HEAD_DIM = 128
BLOCK = 128
REACH = 8


def from_behind(x, axis, by):
    devices = lax.axis_size(axis)
    pairs = [(i, i + by) for i in range(devices) if 0 <= i + by < devices]
    return lax.ppermute(x, axis, pairs)


def fetch_tree(outgoing):
    step1 = from_behind(outgoing[jnp.array([0, 2, 4, 6])], "ctx", 1)
    step2 = from_behind(jnp.stack([outgoing[1], step1[1], outgoing[5], step1[3]]), "ctx", 2)
    step4 = from_behind(jnp.stack([outgoing[3], step1[2], step2[2], step2[3]]), "ctx", 4)
    step8 = from_behind(outgoing[7], "ctx", 8)
    return jnp.stack([step1[0], step2[0], step2[1], step4[0], step4[1], step4[2], step4[3], step8])


def return_tree(sendback):
    step4 = from_behind(sendback[3:7], "ctx", -4)
    step2 = from_behind(jnp.stack([sendback[1], sendback[2], step4[2], step4[3]]), "ctx", -2)
    step1 = from_behind(jnp.stack([sendback[0], step2[1], step4[1], step2[3]]), "ctx", -1)
    step8 = from_behind(sendback[7], "ctx", -8)
    return jnp.stack([step1[0], step2[0], step1[1], step4[0], step1[2], step2[2], step1[3], step8])


def attn_kernel(slot_ref, use_ref, early_ref, q_ref, g_ref, kv_ref, dq_ref, acc_ref, kv_scr, dk_scr, dv_scr,
                *, chosen, group, scaling):
    n = pl.program_id(0)

    @pl.when(n == 0)
    def _():
        acc_ref[...] = jnp.zeros_like(acc_ref)

    keys = chosen * BLOCK
    for e in range(chosen):
        kv_scr[e * BLOCK:(e + 1) * BLOCK, :] = kv_ref[slot_ref[n * chosen + e]]
    key_cat = kv_scr[:, :HEAD_DIM]
    value_cat = kv_scr[:, HEAD_DIM:]

    col = lax.broadcasted_iota(jnp.int32, (BLOCK, keys), 1)
    row = lax.broadcasted_iota(jnp.int32, (BLOCK, keys), 0)
    ent = col // BLOCK
    tok = col % BLOCK
    use_col = jnp.zeros((BLOCK, keys), jnp.int32)
    early_col = jnp.zeros((BLOCK, keys), jnp.int32)
    for e in range(chosen):
        use_col = jnp.where(ent == e, use_ref[n * chosen + e], use_col)
        early_col = jnp.where(ent == e, early_ref[n * chosen + e], early_col)
    allowed = (use_col != 0) & ((early_col != 0) | (tok <= row))

    dk_scr[...] = jnp.zeros_like(dk_scr)
    dv_scr[...] = jnp.zeros_like(dv_scr)
    nt = (((1,), (1,)), ((), ()))
    tn = (((0,), (0,)), ((), ()))
    for h in range(group):
        cols = slice(h * HEAD_DIM, (h + 1) * HEAD_DIM)
        q_h = q_ref[:, cols]
        g_h = g_ref[:, cols]
        scores = lax.dot_general(q_h, key_cat, nt, preferred_element_type=jnp.float32) * scaling
        scores = jnp.where(allowed, scores, -1e30)
        row_max = jnp.max(scores, axis=1, keepdims=True)
        total = jnp.sum(jnp.exp(scores - row_max), axis=1, keepdims=True)
        log_total = row_max + jnp.log(total)
        prob = jnp.exp(scores - log_total)
        prob_half = prob.astype(jnp.bfloat16)
        output = jnp.dot(prob_half, value_cat, preferred_element_type=jnp.float32)
        output = output.astype(jnp.bfloat16).astype(jnp.float32)
        row_dot = jnp.sum(g_h.astype(jnp.float32) * output, axis=1, keepdims=True)
        prob_grad = lax.dot_general(g_h, value_cat, nt, preferred_element_type=jnp.float32)
        score_grad = (prob * (prob_grad - row_dot) * scaling).astype(jnp.bfloat16)
        dq_h = jnp.dot(score_grad, key_cat, preferred_element_type=jnp.float32)
        dq_ref[:, cols] = dq_h.astype(jnp.bfloat16)
        dk_scr[...] += lax.dot_general(score_grad, q_h, tn, preferred_element_type=jnp.float32)
        dv_scr[...] += lax.dot_general(prob_half, g_h, tn, preferred_element_type=jnp.float32)

    for e in range(chosen):
        s = slot_ref[n * chosen + e]
        rows = slice(e * BLOCK, (e + 1) * BLOCK)
        acc_ref[s, :, :HEAD_DIM] += dk_scr[rows, :]
        acc_ref[s, :, HEAD_DIM:] += dv_scr[rows, :]


def attention_terms(slots, usable, earlier, query_states, out_grad, kv_stock, chosen):
    tok_rows, q_cols = query_states.shape
    slot_count = kv_stock.shape[0]
    group = q_cols // HEAD_DIM
    blocks_here = tok_rows // BLOCK
    kernel = functools.partial(attn_kernel, chosen=chosen, group=group, scaling=1.0 / math.sqrt(HEAD_DIM))
    grid_spec = pltpu.PrefetchScalarGridSpec(
        num_scalar_prefetch=3,
        grid=(blocks_here,),
        in_specs=[
            pl.BlockSpec((BLOCK, q_cols), lambda n, *_: (n, 0)),
            pl.BlockSpec((BLOCK, q_cols), lambda n, *_: (n, 0)),
            pl.BlockSpec((slot_count, BLOCK, 2 * HEAD_DIM), lambda n, *_: (0, 0, 0)),
        ],
        out_specs=[
            pl.BlockSpec((BLOCK, q_cols), lambda n, *_: (n, 0)),
            pl.BlockSpec((slot_count, BLOCK, 2 * HEAD_DIM), lambda n, *_: (0, 0, 0)),
        ],
        scratch_shapes=[
            pltpu.VMEM((chosen * BLOCK, 2 * HEAD_DIM), jnp.bfloat16),
            pltpu.VMEM((chosen * BLOCK, HEAD_DIM), jnp.float32),
            pltpu.VMEM((chosen * BLOCK, HEAD_DIM), jnp.float32),
        ],
    )
    return pl.pallas_call(
        kernel,
        grid_spec=grid_spec,
        out_shape=[
            jax.ShapeDtypeStruct((tok_rows, q_cols), jnp.bfloat16),
            jax.ShapeDtypeStruct((slot_count, BLOCK, 2 * HEAD_DIM), jnp.float32),
        ],
        compiler_params=pltpu.CompilerParams(dimension_semantics=("arbitrary",)),
    )(slots, usable, earlier, query_states, out_grad, kv_stock)


def body(query_states, key_states, value_states, out_grad, block_lists):
    ctx_count = lax.axis_size("ctx")
    head_count = lax.axis_size("head")
    myself = lax.axis_index("ctx")
    tok_rows = query_states.shape[0]
    kv_cols = key_states.shape[1]
    blocks_here = tok_rows // BLOCK
    chosen = block_lists.shape[1]
    lists_by_dev = block_lists.reshape(ctx_count, blocks_here * chosen)
    slot_ids = jnp.arange(blocks_here, dtype=jnp.int32)
    distances = jnp.arange(1, REACH + 1, dtype=jnp.int32)
    targets = myself + distances
    target_ok = targets < ctx_count
    target_rows = jnp.take(lists_by_dev, jnp.minimum(targets, ctx_count - 1), axis=0)
    mine = target_rows // blocks_here == myself
    requested = jnp.max(jnp.where(mine, target_rows % blocks_here, -1), axis=1)
    requested = jnp.where(target_ok, requested, -1)
    kv_local = jnp.concatenate([key_states, value_states], axis=1).reshape(blocks_here, BLOCK, 2 * kv_cols)
    outgoing = jnp.take(kv_local, jnp.clip(requested, 0, blocks_here - 1), axis=0)
    kv_stock = jnp.concatenate([kv_local, fetch_tree(outgoing)], axis=0)

    own_entries = lax.dynamic_slice_in_dim(block_lists, myself * blocks_here, blocks_here, 0)
    block_ids = myself * blocks_here + slot_ids
    order_ids = jnp.arange(chosen, dtype=jnp.int32)
    repeat = (own_entries[:, :, None] == own_entries[:, None, :]) & (
        order_ids[None, None, :] < order_ids[None, :, None]
    )
    usable = jnp.logical_not(jnp.any(repeat, axis=2))
    earlier = own_entries < block_ids[:, None]
    behind = myself - own_entries // blocks_here
    slots = jnp.where(behind == 0, own_entries % blocks_here, blocks_here - 1 + behind)
    slots = jnp.clip(slots, 0, blocks_here + REACH - 1)

    query_local, acc = attention_terms(
        slots.reshape(-1).astype(jnp.int32),
        usable.reshape(-1).astype(jnp.int32),
        earlier.reshape(-1).astype(jnp.int32),
        query_states,
        out_grad,
        kv_stock,
        chosen,
    )
    sendback = acc[blocks_here:].astype(jnp.bfloat16)
    arrived = return_tree(sendback).astype(jnp.float32)
    credit = (requested[None, :] == slot_ids[:, None]).astype(jnp.float32)
    totals = acc[:blocks_here] + jnp.sum(credit[:, :, None, None] * arrived[None], axis=1)
    kv_grad = totals.reshape(tok_rows, 2 * kv_cols).astype(jnp.bfloat16)
    q_cols = query_local.shape[1]
    both = jnp.concatenate([query_local, kv_grad], axis=1)
    both = lax.all_to_all(both, "head", split_axis=0, concat_axis=1, tiled=True)
    both = both.reshape(tok_rows // head_count, head_count, q_cols + 2 * kv_cols)
    out_rows = tok_rows // head_count
    query_grad = both[:, :, :q_cols].reshape(out_rows, head_count * q_cols)
    key_grad = both[:, :, q_cols:q_cols + kv_cols].reshape(out_rows, head_count * kv_cols)
    value_grad = both[:, :, q_cols + kv_cols:].reshape(out_rows, head_count * kv_cols)
    return (query_grad, key_grad, value_grad)


def solution(mesh):
    in_specs = (P("ctx", "head"), P("ctx", "head"), P("ctx", "head"), P("ctx", "head"), P())
    out_specs = (P(("ctx", "head"), None), P(("ctx", "head"), None), P(("ctx", "head"), None))
    return jax.shard_map(body, mesh=mesh, in_specs=in_specs, out_specs=out_specs, check_vma=False)
```

```python
import functools
import math

import jax
import jax.numpy as jnp
from jax import lax
from jax.experimental import pallas as pl
from jax.experimental.pallas import tpu as pltpu
from jax.sharding import PartitionSpec as P

HEADS = 64
KV_HEADS = 8
HEAD_DIM = 128
BLOCK = 128
REACH = 8


def from_behind(x, axis, by):
    devices = lax.axis_size(axis)
    pairs = [(i, i + by) for i in range(devices) if 0 <= i + by < devices]
    return lax.ppermute(x, axis, pairs)


def fetch_tree(outgoing):
    step1 = from_behind(outgoing[jnp.array([0, 2, 4, 6])], "ctx", 1)
    step2 = from_behind(jnp.stack([outgoing[1], step1[1], outgoing[5], step1[3]]), "ctx", 2)
    step4 = from_behind(jnp.stack([outgoing[3], step1[2], step2[2], step2[3]]), "ctx", 4)
    step8 = from_behind(outgoing[7], "ctx", 8)
    return jnp.stack([step1[0], step2[0], step2[1], step4[0], step4[1], step4[2], step4[3], step8])


def return_tree(sendback):
    step4 = from_behind(sendback[3:7], "ctx", -4)
    step2 = from_behind(jnp.stack([sendback[1], sendback[2], step4[2], step4[3]]), "ctx", -2)
    step1 = from_behind(jnp.stack([sendback[0], step2[1], step4[1], step2[3]]), "ctx", -1)
    step8 = from_behind(sendback[7], "ctx", -8)
    return jnp.stack([step1[0], step2[0], step1[1], step4[0], step1[2], step2[2], step1[3], step8])


def attn_kernel(slot_ref, use_ref, early_ref, q_ref, g_ref, kv_ref, dq_ref, acc_ref, kv_scr, qs_scr, gs_scr,
                *, chosen, group, scaling):
    n = pl.program_id(0)

    @pl.when(n == 0)
    def _():
        acc_ref[...] = jnp.zeros_like(acc_ref)

    keys = chosen * BLOCK
    for e in range(chosen):
        kv_scr[e * BLOCK:(e + 1) * BLOCK, :] = kv_ref[slot_ref[n * chosen + e]]
    key_cat = kv_scr[:, :HEAD_DIM]
    value_cat = kv_scr[:, HEAD_DIM:]
    for h in range(group):
        qs_scr[h * BLOCK:(h + 1) * BLOCK, :] = q_ref[:, h * HEAD_DIM:(h + 1) * HEAD_DIM]
        gs_scr[h * BLOCK:(h + 1) * BLOCK, :] = g_ref[:, h * HEAD_DIM:(h + 1) * HEAD_DIM]
    q_all = qs_scr[...]
    g_all = gs_scr[...]

    col = lax.broadcasted_iota(jnp.int32, (BLOCK, keys), 1)
    row = lax.broadcasted_iota(jnp.int32, (BLOCK, keys), 0)
    ent = col // BLOCK
    tok = col % BLOCK
    use_col = jnp.zeros((BLOCK, keys), jnp.int32)
    early_col = jnp.zeros((BLOCK, keys), jnp.int32)
    for e in range(chosen):
        use_col = jnp.where(ent == e, use_ref[n * chosen + e], use_col)
        early_col = jnp.where(ent == e, early_ref[n * chosen + e], early_col)
    allowed = (use_col != 0) & ((early_col != 0) | (tok <= row))

    nt = (((1,), (1,)), ((), ()))
    tn = (((0,), (0,)), ((), ()))
    rows = group * BLOCK
    scores = lax.dot_general(q_all, key_cat, nt, preferred_element_type=jnp.float32) * scaling
    scores = scores.reshape(group, BLOCK, keys)
    scores = jnp.where(allowed[None], scores, -1e30)
    row_max = jnp.max(scores, axis=2, keepdims=True)
    total = jnp.sum(jnp.exp(scores - row_max), axis=2, keepdims=True)
    log_total = row_max + jnp.log(total)
    prob = jnp.exp(scores - log_total).reshape(rows, keys)
    prob_half = prob.astype(jnp.bfloat16)
    output = jnp.dot(prob_half, value_cat, preferred_element_type=jnp.float32)
    output = output.astype(jnp.bfloat16).astype(jnp.float32)
    row_dot = jnp.sum(g_all.astype(jnp.float32) * output, axis=1, keepdims=True)
    prob_grad = lax.dot_general(g_all, value_cat, nt, preferred_element_type=jnp.float32)
    score_grad = (prob * (prob_grad - row_dot) * scaling).astype(jnp.bfloat16)
    dq_all = jnp.dot(score_grad, key_cat, preferred_element_type=jnp.float32).astype(jnp.bfloat16)
    for h in range(group):
        dq_ref[:, h * HEAD_DIM:(h + 1) * HEAD_DIM] = dq_all[h * BLOCK:(h + 1) * BLOCK, :]
    key_t = lax.dot_general(q_all, score_grad, tn, preferred_element_type=jnp.float32)
    value_t = lax.dot_general(g_all, prob_half, tn, preferred_element_type=jnp.float32)
    key_part = key_t.T
    value_part = value_t.T

    for e in range(chosen):
        s = slot_ref[n * chosen + e]
        part = slice(e * BLOCK, (e + 1) * BLOCK)
        acc_ref[s, :, :HEAD_DIM] += key_part[part, :]
        acc_ref[s, :, HEAD_DIM:] += value_part[part, :]


def attention_terms(slots, usable, earlier, query_states, out_grad, kv_stock, chosen):
    tok_rows, q_cols = query_states.shape
    slot_count = kv_stock.shape[0]
    group = q_cols // HEAD_DIM
    blocks_here = tok_rows // BLOCK
    kernel = functools.partial(attn_kernel, chosen=chosen, group=group, scaling=1.0 / math.sqrt(HEAD_DIM))
    grid_spec = pltpu.PrefetchScalarGridSpec(
        num_scalar_prefetch=3,
        grid=(blocks_here,),
        in_specs=[
            pl.BlockSpec((BLOCK, q_cols), lambda n, *_: (n, 0)),
            pl.BlockSpec((BLOCK, q_cols), lambda n, *_: (n, 0)),
            pl.BlockSpec((slot_count, BLOCK, 2 * HEAD_DIM), lambda n, *_: (0, 0, 0)),
        ],
        out_specs=[
            pl.BlockSpec((BLOCK, q_cols), lambda n, *_: (n, 0)),
            pl.BlockSpec((slot_count, BLOCK, 2 * HEAD_DIM), lambda n, *_: (0, 0, 0)),
        ],
        scratch_shapes=[
            pltpu.VMEM((chosen * BLOCK, 2 * HEAD_DIM), jnp.bfloat16),
            pltpu.VMEM((group * BLOCK, HEAD_DIM), jnp.bfloat16),
            pltpu.VMEM((group * BLOCK, HEAD_DIM), jnp.bfloat16),
        ],
    )
    return pl.pallas_call(
        kernel,
        grid_spec=grid_spec,
        out_shape=[
            jax.ShapeDtypeStruct((tok_rows, q_cols), jnp.bfloat16),
            jax.ShapeDtypeStruct((slot_count, BLOCK, 2 * HEAD_DIM), jnp.float32),
        ],
        compiler_params=pltpu.CompilerParams(dimension_semantics=("arbitrary",)),
    )(slots, usable, earlier, query_states, out_grad, kv_stock)


def body(query_states, key_states, value_states, out_grad, block_lists):
    ctx_count = lax.axis_size("ctx")
    head_count = lax.axis_size("head")
    myself = lax.axis_index("ctx")
    tok_rows = query_states.shape[0]
    kv_cols = key_states.shape[1]
    blocks_here = tok_rows // BLOCK
    chosen = block_lists.shape[1]
    lists_by_dev = block_lists.reshape(ctx_count, blocks_here * chosen)
    slot_ids = jnp.arange(blocks_here, dtype=jnp.int32)
    distances = jnp.arange(1, REACH + 1, dtype=jnp.int32)
    targets = myself + distances
    target_ok = targets < ctx_count
    target_rows = jnp.take(lists_by_dev, jnp.minimum(targets, ctx_count - 1), axis=0)
    mine = target_rows // blocks_here == myself
    requested = jnp.max(jnp.where(mine, target_rows % blocks_here, -1), axis=1)
    requested = jnp.where(target_ok, requested, -1)
    kv_local = jnp.concatenate([key_states, value_states], axis=1).reshape(blocks_here, BLOCK, 2 * kv_cols)
    outgoing = jnp.take(kv_local, jnp.clip(requested, 0, blocks_here - 1), axis=0)
    kv_stock = jnp.concatenate([kv_local, fetch_tree(outgoing)], axis=0)

    own_entries = lax.dynamic_slice_in_dim(block_lists, myself * blocks_here, blocks_here, 0)
    block_ids = myself * blocks_here + slot_ids
    order_ids = jnp.arange(chosen, dtype=jnp.int32)
    repeat = (own_entries[:, :, None] == own_entries[:, None, :]) & (
        order_ids[None, None, :] < order_ids[None, :, None]
    )
    usable = jnp.logical_not(jnp.any(repeat, axis=2))
    earlier = own_entries < block_ids[:, None]
    behind = myself - own_entries // blocks_here
    slots = jnp.where(behind == 0, own_entries % blocks_here, blocks_here - 1 + behind)
    slots = jnp.clip(slots, 0, blocks_here + REACH - 1)

    query_local, acc = attention_terms(
        slots.reshape(-1).astype(jnp.int32),
        usable.reshape(-1).astype(jnp.int32),
        earlier.reshape(-1).astype(jnp.int32),
        query_states,
        out_grad,
        kv_stock,
        chosen,
    )
    sendback = acc[blocks_here:].astype(jnp.bfloat16)
    arrived = return_tree(sendback).astype(jnp.float32)
    credit = (requested[None, :] == slot_ids[:, None]).astype(jnp.float32)
    totals = acc[:blocks_here] + jnp.sum(credit[:, :, None, None] * arrived[None], axis=1)
    kv_grad = totals.reshape(tok_rows, 2 * kv_cols).astype(jnp.bfloat16)
    q_cols = query_local.shape[1]
    both = jnp.concatenate([query_local, kv_grad], axis=1)
    both = lax.all_to_all(both, "head", split_axis=0, concat_axis=1, tiled=True)
    both = both.reshape(tok_rows // head_count, head_count, q_cols + 2 * kv_cols)
    out_rows = tok_rows // head_count
    query_grad = both[:, :, :q_cols].reshape(out_rows, head_count * q_cols)
    key_grad = both[:, :, q_cols:q_cols + kv_cols].reshape(out_rows, head_count * kv_cols)
    value_grad = both[:, :, q_cols + kv_cols:].reshape(out_rows, head_count * kv_cols)
    return (query_grad, key_grad, value_grad)


def solution(mesh):
    in_specs = (P("ctx", "head"), P("ctx", "head"), P("ctx", "head"), P("ctx", "head"), P())
    out_specs = (P(("ctx", "head"), None), P(("ctx", "head"), None), P(("ctx", "head"), None))
    return jax.shard_map(body, mesh=mesh, in_specs=in_specs, out_specs=out_specs, check_vma=False)
```

```python
import functools
import math

import jax
import jax.numpy as jnp
from jax import lax
from jax.experimental import pallas as pl
from jax.experimental.pallas import tpu as pltpu
from jax.sharding import PartitionSpec as P


HEAD_DIM = 128
BLOCK = 128
REACH = 8


def from_behind(x, axis, by):
    devices = lax.axis_size(axis)
    pairs = [(i, i + by) for i in range(devices) if 0 <= i + by < devices]
    return lax.ppermute(x, axis, pairs)


def fetch_tree(outgoing):
    step1 = from_behind(outgoing[jnp.array([0, 2, 4, 6])], "ctx", 1)
    step2 = from_behind(jnp.stack([outgoing[1], step1[1], outgoing[5], step1[3]]), "ctx", 2)
    step4 = from_behind(jnp.stack([outgoing[3], step1[2], step2[2], step2[3]]), "ctx", 4)
    step8 = from_behind(outgoing[7], "ctx", 8)
    return jnp.stack([step1[0], step2[0], step2[1], step4[0], step4[1], step4[2], step4[3], step8])


def return_tree(sendback):
    step4 = from_behind(sendback[3:7], "ctx", -4)
    step2 = from_behind(jnp.stack([sendback[1], sendback[2], step4[2], step4[3]]), "ctx", -2)
    step1 = from_behind(jnp.stack([sendback[0], step2[1], step4[1], step2[3]]), "ctx", -1)
    step8 = from_behind(sendback[7], "ctx", -8)
    return jnp.stack([step1[0], step2[0], step1[1], step4[0], step1[2], step2[2], step1[3], step8])


def attn_kernel(slot_ref, use_ref, early_ref, q_ref, g_ref, kv_ref, dq_ref, acc_ref, kv_scr, qs_scr, gs_scr,
                *, chosen, group, scaling):
    n = pl.program_id(0)

    @pl.when(n == 0)
    def _():
        acc_ref[...] = jnp.zeros_like(acc_ref)

    keys = chosen * BLOCK
    for e in range(chosen):
        kv_scr[e * BLOCK:(e + 1) * BLOCK, :] = kv_ref[slot_ref[n * chosen + e]]
    key_cat = kv_scr[:, :HEAD_DIM]
    value_cat = kv_scr[:, HEAD_DIM:]
    for h in range(group):
        qs_scr[h * BLOCK:(h + 1) * BLOCK, :] = q_ref[:, h * HEAD_DIM:(h + 1) * HEAD_DIM]
        gs_scr[h * BLOCK:(h + 1) * BLOCK, :] = g_ref[:, h * HEAD_DIM:(h + 1) * HEAD_DIM]
    q_all = qs_scr[...]
    g_all = gs_scr[...]

    col = lax.broadcasted_iota(jnp.int32, (BLOCK, keys), 1)
    row = lax.broadcasted_iota(jnp.int32, (BLOCK, keys), 0)
    ent = col // BLOCK
    tok = col % BLOCK
    use_col = jnp.zeros((BLOCK, keys), jnp.int32)
    early_col = jnp.zeros((BLOCK, keys), jnp.int32)
    for e in range(chosen):
        use_col = jnp.where(ent == e, use_ref[n * chosen + e], use_col)
        early_col = jnp.where(ent == e, early_ref[n * chosen + e], early_col)
    allowed = (use_col != 0) & ((early_col != 0) | (tok <= row))

    nt = (((1,), (1,)), ((), ()))
    tn = (((0,), (0,)), ((), ()))
    rows = group * BLOCK
    scores = lax.dot_general(q_all, key_cat, nt, preferred_element_type=jnp.float32) * scaling
    scores = scores.reshape(group, BLOCK, keys)
    scores = jnp.where(allowed[None], scores, -1e30)
    row_max = jnp.max(scores, axis=2, keepdims=True)
    total = jnp.sum(jnp.exp(scores - row_max), axis=2, keepdims=True)
    log_total = row_max + jnp.log(total)
    prob = jnp.exp(scores - log_total).reshape(rows, keys)
    prob_half = prob.astype(jnp.bfloat16)
    output = jnp.dot(prob_half, value_cat, preferred_element_type=jnp.float32)
    output = output.astype(jnp.bfloat16).astype(jnp.float32)
    row_dot = jnp.sum(g_all.astype(jnp.float32) * output, axis=1, keepdims=True)
    prob_grad = lax.dot_general(g_all, value_cat, nt, preferred_element_type=jnp.float32)
    score_grad = (prob * (prob_grad - row_dot) * scaling).astype(jnp.bfloat16)
    dq_all = jnp.dot(score_grad, key_cat, preferred_element_type=jnp.float32).astype(jnp.bfloat16)
    for h in range(group):
        dq_ref[:, h * HEAD_DIM:(h + 1) * HEAD_DIM] = dq_all[h * BLOCK:(h + 1) * BLOCK, :]
    key_t = lax.dot_general(q_all, score_grad, tn, preferred_element_type=jnp.float32)
    value_t = lax.dot_general(g_all, prob_half, tn, preferred_element_type=jnp.float32)
    key_part = key_t.T
    value_part = value_t.T

    for e in range(chosen):
        s = slot_ref[n * chosen + e]
        part = slice(e * BLOCK, (e + 1) * BLOCK)
        acc_ref[s, :, :HEAD_DIM] += key_part[part, :]
        acc_ref[s, :, HEAD_DIM:] += value_part[part, :]


def attention_terms(slots, usable, earlier, query_states, out_grad, kv_stock, chosen):
    tok_rows, q_cols = query_states.shape
    slot_count = kv_stock.shape[0]
    group = q_cols // HEAD_DIM
    blocks_here = tok_rows // BLOCK
    kernel = functools.partial(attn_kernel, chosen=chosen, group=group, scaling=1.0 / math.sqrt(HEAD_DIM))
    grid_spec = pltpu.PrefetchScalarGridSpec(
        num_scalar_prefetch=3,
        grid=(blocks_here,),
        in_specs=[
            pl.BlockSpec((BLOCK, q_cols), lambda n, *_: (n, 0)),
            pl.BlockSpec((BLOCK, q_cols), lambda n, *_: (n, 0)),
            pl.BlockSpec((slot_count, BLOCK, 2 * HEAD_DIM), lambda n, *_: (0, 0, 0)),
        ],
        out_specs=[
            pl.BlockSpec((BLOCK, q_cols), lambda n, *_: (n, 0)),
            pl.BlockSpec((slot_count, BLOCK, 2 * HEAD_DIM), lambda n, *_: (0, 0, 0)),
        ],
        scratch_shapes=[
            pltpu.VMEM((chosen * BLOCK, 2 * HEAD_DIM), jnp.bfloat16),
            pltpu.VMEM((group * BLOCK, HEAD_DIM), jnp.bfloat16),
            pltpu.VMEM((group * BLOCK, HEAD_DIM), jnp.bfloat16),
        ],
    )
    return pl.pallas_call(
        kernel,
        grid_spec=grid_spec,
        out_shape=[
            jax.ShapeDtypeStruct((tok_rows, q_cols), jnp.bfloat16),
            jax.ShapeDtypeStruct((slot_count, BLOCK, 2 * HEAD_DIM), jnp.float32),
        ],
        compiler_params=pltpu.CompilerParams(dimension_semantics=("arbitrary",)),
    )(slots, usable, earlier, query_states, out_grad, kv_stock)


def step(query_states, key_states, value_states, out_grad, block_lists):
    ctx_count = lax.axis_size("ctx")
    head_count = lax.axis_size("head")
    myself = lax.axis_index("ctx")
    tok_rows = query_states.shape[0]
    kv_cols = key_states.shape[1]
    blocks_here = tok_rows // BLOCK
    chosen = block_lists.shape[1]
    lists_by_dev = block_lists.reshape(ctx_count, blocks_here * chosen)
    slot_ids = jnp.arange(blocks_here, dtype=jnp.int32)
    distances = jnp.arange(1, REACH + 1, dtype=jnp.int32)
    targets = myself + distances
    target_ok = targets < ctx_count
    target_rows = jnp.take(lists_by_dev, jnp.minimum(targets, ctx_count - 1), axis=0)
    mine = target_rows // blocks_here == myself
    requested = jnp.max(jnp.where(mine, target_rows % blocks_here, -1), axis=1)
    requested = jnp.where(target_ok, requested, -1)
    kv_local = jnp.concatenate([key_states, value_states], axis=1).reshape(blocks_here, BLOCK, 2 * kv_cols)
    outgoing = jnp.take(kv_local, jnp.clip(requested, 0, blocks_here - 1), axis=0)
    kv_stock = jnp.concatenate([kv_local, fetch_tree(outgoing)], axis=0)

    own_entries = lax.dynamic_slice_in_dim(block_lists, myself * blocks_here, blocks_here, 0)
    block_ids = myself * blocks_here + slot_ids
    order_ids = jnp.arange(chosen, dtype=jnp.int32)
    repeat = (own_entries[:, :, None] == own_entries[:, None, :]) & (
        order_ids[None, None, :] < order_ids[None, :, None]
    )
    usable = jnp.logical_not(jnp.any(repeat, axis=2))
    earlier = own_entries < block_ids[:, None]
    behind = myself - own_entries // blocks_here
    slots = jnp.where(behind == 0, own_entries % blocks_here, blocks_here - 1 + behind)
    slots = jnp.clip(slots, 0, blocks_here + REACH - 1)

    query_local, acc = attention_terms(
        slots.reshape(-1).astype(jnp.int32),
        usable.reshape(-1).astype(jnp.int32),
        earlier.reshape(-1).astype(jnp.int32),
        query_states,
        out_grad,
        kv_stock,
        chosen,
    )
    query_grad = lax.all_to_all(query_local, "head", split_axis=0, concat_axis=1, tiled=True)
    sendback = acc[blocks_here:].astype(jnp.bfloat16)
    arrived = return_tree(sendback).astype(jnp.float32)
    credit = (requested[None, :] == slot_ids[:, None]).astype(jnp.float32)
    totals = acc[:blocks_here] + jnp.sum(credit[:, :, None, None] * arrived[None], axis=1)
    kv_grad = totals.reshape(tok_rows, 2 * kv_cols).astype(jnp.bfloat16)
    kv_all = lax.all_to_all(kv_grad, "head", split_axis=0, concat_axis=1, tiled=True)
    out_rows = tok_rows // head_count
    kv_all = kv_all.reshape(out_rows, head_count, 2, kv_cols)
    key_grad = kv_all[:, :, 0, :].reshape(out_rows, head_count * kv_cols)
    value_grad = kv_all[:, :, 1, :].reshape(out_rows, head_count * kv_cols)
    return (query_grad, key_grad, value_grad)


def solution(mesh):
    in_specs = (P("ctx", "head"), P("ctx", "head"), P("ctx", "head"), P("ctx", "head"), P())
    out_specs = (P(("ctx", "head"), None), P(("ctx", "head"), None), P(("ctx", "head"), None))
    return jax.shard_map(step, mesh=mesh, in_specs=in_specs, out_specs=out_specs, check_vma=False)
```

```python
import functools
import math

import jax
import jax.numpy as jnp
from jax import lax
from jax.experimental import pallas as pl
from jax.experimental.pallas import tpu as pltpu
from jax.sharding import PartitionSpec as P


HEAD_DIM = 128
BLOCK = 128
REACH = 8


def from_behind(x, axis, by):
    devices = lax.axis_size(axis)
    pairs = [(i, i + by) for i in range(devices) if 0 <= i + by < devices]
    return lax.ppermute(x, axis, pairs)


def fetch_tree(outgoing):
    step1 = from_behind(outgoing[jnp.array([0, 2, 4, 6])], "ctx", 1)
    step2 = from_behind(jnp.stack([outgoing[1], step1[1], outgoing[5], step1[3]]), "ctx", 2)
    step4 = from_behind(jnp.stack([outgoing[3], step1[2], step2[2], step2[3]]), "ctx", 4)
    step8 = from_behind(outgoing[7], "ctx", 8)
    return jnp.stack([step1[0], step2[0], step2[1], step4[0], step4[1], step4[2], step4[3], step8])


def return_tree(sendback):
    step4 = from_behind(sendback[3:7], "ctx", -4)
    step2 = from_behind(jnp.stack([sendback[1], sendback[2], step4[2], step4[3]]), "ctx", -2)
    step1 = from_behind(jnp.stack([sendback[0], step2[1], step4[1], step2[3]]), "ctx", -1)
    step8 = from_behind(sendback[7], "ctx", -8)
    return jnp.stack([step1[0], step2[0], step1[1], step4[0], step1[2], step2[2], step1[3], step8])


def attn_kernel(slot_ref, use_ref, early_ref, q_ref, g_ref, kv_ref, dq_ref, home_ref, away_ref, kv_scr, qs_scr, gs_scr,
                acc_ref, *, chosen, group, scaling):
    n = pl.program_id(0)
    homes = home_ref.shape[0]

    @pl.when(n == 0)
    def _():
        acc_ref[...] = jnp.zeros_like(acc_ref)

    keys = chosen * BLOCK
    for e in range(chosen):
        kv_scr[e * BLOCK:(e + 1) * BLOCK, :] = kv_ref[slot_ref[n * chosen + e]]
    key_cat = kv_scr[:, :HEAD_DIM]
    value_cat = kv_scr[:, HEAD_DIM:]
    for h in range(group):
        qs_scr[h * BLOCK:(h + 1) * BLOCK, :] = q_ref[:, h * HEAD_DIM:(h + 1) * HEAD_DIM]
        gs_scr[h * BLOCK:(h + 1) * BLOCK, :] = g_ref[:, h * HEAD_DIM:(h + 1) * HEAD_DIM]
    q_all = qs_scr[...]
    g_all = gs_scr[...]

    col = lax.broadcasted_iota(jnp.int32, (BLOCK, keys), 1)
    row = lax.broadcasted_iota(jnp.int32, (BLOCK, keys), 0)
    ent = col // BLOCK
    tok = col % BLOCK
    use_col = jnp.zeros((BLOCK, keys), jnp.int32)
    early_col = jnp.zeros((BLOCK, keys), jnp.int32)
    for e in range(chosen):
        use_col = jnp.where(ent == e, use_ref[n * chosen + e], use_col)
        early_col = jnp.where(ent == e, early_ref[n * chosen + e], early_col)
    allowed = (use_col != 0) & ((early_col != 0) | (tok <= row))

    nt = (((1,), (1,)), ((), ()))
    tn = (((0,), (0,)), ((), ()))
    rows = group * BLOCK
    scores = lax.dot_general(q_all, key_cat, nt, preferred_element_type=jnp.float32) * scaling
    scores = scores.reshape(group, BLOCK, keys)
    scores = jnp.where(allowed[None], scores, -1e30)
    row_max = jnp.max(scores, axis=2, keepdims=True)
    total = jnp.sum(jnp.exp(scores - row_max), axis=2, keepdims=True)
    log_total = row_max + jnp.log(total)
    prob = jnp.exp(scores - log_total).reshape(rows, keys)
    prob_half = prob.astype(jnp.bfloat16)
    output = jnp.dot(prob_half, value_cat, preferred_element_type=jnp.float32)
    output = output.astype(jnp.bfloat16).astype(jnp.float32)
    row_dot = jnp.sum(g_all.astype(jnp.float32) * output, axis=1, keepdims=True)
    prob_grad = lax.dot_general(g_all, value_cat, nt, preferred_element_type=jnp.float32)
    score_grad = (prob * (prob_grad - row_dot) * scaling).astype(jnp.bfloat16)
    dq_all = jnp.dot(score_grad, key_cat, preferred_element_type=jnp.float32).astype(jnp.bfloat16)
    for h in range(group):
        dq_ref[:, h * HEAD_DIM:(h + 1) * HEAD_DIM] = dq_all[h * BLOCK:(h + 1) * BLOCK, :]
    key_t = lax.dot_general(q_all, score_grad, tn, preferred_element_type=jnp.float32)
    value_t = lax.dot_general(g_all, prob_half, tn, preferred_element_type=jnp.float32)
    key_part = key_t.T
    value_part = value_t.T

    for e in range(chosen):
        s = slot_ref[n * chosen + e]
        part = slice(e * BLOCK, (e + 1) * BLOCK)
        acc_ref[s, :, :HEAD_DIM] += key_part[part, :]
        acc_ref[s, :, HEAD_DIM:] += value_part[part, :]

    @pl.when(n == pl.num_programs(0) - 1)
    def _():
        home_ref[...] = acc_ref[:homes]
        away_ref[...] = acc_ref[homes:].astype(jnp.bfloat16)


def attention_terms(slots, usable, earlier, query_states, out_grad, kv_stock, chosen):
    tok_rows, q_cols = query_states.shape
    slot_count = kv_stock.shape[0]
    group = q_cols // HEAD_DIM
    blocks_here = tok_rows // BLOCK
    kernel = functools.partial(attn_kernel, chosen=chosen, group=group, scaling=1.0 / math.sqrt(HEAD_DIM))
    grid_spec = pltpu.PrefetchScalarGridSpec(
        num_scalar_prefetch=3,
        grid=(blocks_here,),
        in_specs=[
            pl.BlockSpec((BLOCK, q_cols), lambda n, *_: (n, 0)),
            pl.BlockSpec((BLOCK, q_cols), lambda n, *_: (n, 0)),
            pl.BlockSpec((slot_count, BLOCK, 2 * HEAD_DIM), lambda n, *_: (0, 0, 0)),
        ],
        out_specs=[
            pl.BlockSpec((BLOCK, q_cols), lambda n, *_: (n, 0)),
            pl.BlockSpec((blocks_here, BLOCK, 2 * HEAD_DIM), lambda n, *_: (0, 0, 0)),
            pl.BlockSpec((slot_count - blocks_here, BLOCK, 2 * HEAD_DIM), lambda n, *_: (0, 0, 0)),
        ],
        scratch_shapes=[
            pltpu.VMEM((chosen * BLOCK, 2 * HEAD_DIM), jnp.bfloat16),
            pltpu.VMEM((group * BLOCK, HEAD_DIM), jnp.bfloat16),
            pltpu.VMEM((group * BLOCK, HEAD_DIM), jnp.bfloat16),
            pltpu.VMEM((slot_count, BLOCK, 2 * HEAD_DIM), jnp.float32),
        ],
    )
    return pl.pallas_call(
        kernel,
        grid_spec=grid_spec,
        out_shape=[
            jax.ShapeDtypeStruct((tok_rows, q_cols), jnp.bfloat16),
            jax.ShapeDtypeStruct((blocks_here, BLOCK, 2 * HEAD_DIM), jnp.float32),
            jax.ShapeDtypeStruct((slot_count - blocks_here, BLOCK, 2 * HEAD_DIM), jnp.bfloat16),
        ],
        compiler_params=pltpu.CompilerParams(dimension_semantics=("arbitrary",)),
    )(slots, usable, earlier, query_states, out_grad, kv_stock)


def step(query_states, key_states, value_states, out_grad, block_lists):
    ctx_count = lax.axis_size("ctx")
    head_count = lax.axis_size("head")
    myself = lax.axis_index("ctx")
    tok_rows = query_states.shape[0]
    kv_cols = key_states.shape[1]
    blocks_here = tok_rows // BLOCK
    chosen = block_lists.shape[1]
    lists_by_dev = block_lists.reshape(ctx_count, blocks_here * chosen)
    slot_ids = jnp.arange(blocks_here, dtype=jnp.int32)
    no_rows = jnp.full((REACH, blocks_here * chosen), -blocks_here, jnp.int32)
    lists_pad = jnp.concatenate([lists_by_dev, no_rows], axis=0)
    target_rows = lax.dynamic_slice_in_dim(lists_pad, myself + 1, REACH, 0)
    mine = target_rows // blocks_here == myself
    requested = jnp.max(jnp.where(mine, target_rows % blocks_here, -1), axis=1)
    kv_local = jnp.concatenate([key_states, value_states], axis=1).reshape(blocks_here, BLOCK, 2 * kv_cols)
    outgoing = jnp.take(kv_local, jnp.clip(requested, 0, blocks_here - 1), axis=0)
    kv_stock = jnp.concatenate([kv_local, fetch_tree(outgoing)], axis=0)

    own_entries = lax.dynamic_slice_in_dim(block_lists, myself * blocks_here, blocks_here, 0)
    block_ids = myself * blocks_here + slot_ids
    order_ids = jnp.arange(chosen, dtype=jnp.int32)
    repeat = (own_entries[:, :, None] == own_entries[:, None, :]) & (
        order_ids[None, None, :] < order_ids[None, :, None]
    )
    usable = jnp.logical_not(jnp.any(repeat, axis=2))
    earlier = own_entries < block_ids[:, None]
    behind = myself - own_entries // blocks_here
    slots = jnp.where(behind == 0, own_entries % blocks_here, blocks_here - 1 + behind)
    slots = jnp.clip(slots, 0, blocks_here + REACH - 1)

    query_local, home, away = attention_terms(
        slots.reshape(-1).astype(jnp.int32),
        usable.reshape(-1).astype(jnp.int32),
        earlier.reshape(-1).astype(jnp.int32),
        query_states,
        out_grad,
        kv_stock,
        chosen,
    )
    query_grad = lax.all_to_all(query_local, "head", split_axis=0, concat_axis=1, tiled=True)
    arrived = return_tree(away).astype(jnp.float32)
    credit = (requested[None, :] == slot_ids[:, None]).astype(jnp.float32)
    totals = home + jnp.sum(credit[:, :, None, None] * arrived[None], axis=1)
    kv_grad = totals.reshape(tok_rows, 2 * kv_cols).astype(jnp.bfloat16)
    kv_all = lax.all_to_all(kv_grad, "head", split_axis=0, concat_axis=1, tiled=True)
    out_rows = tok_rows // head_count
    kv_all = kv_all.reshape(out_rows, head_count, 2, kv_cols)
    key_grad = kv_all[:, :, 0, :].reshape(out_rows, head_count * kv_cols)
    value_grad = kv_all[:, :, 1, :].reshape(out_rows, head_count * kv_cols)
    return (query_grad, key_grad, value_grad)


def solution(mesh):
    in_specs = (P("ctx", "head"), P("ctx", "head"), P("ctx", "head"), P("ctx", "head"), P())
    out_specs = (P(("ctx", "head"), None), P(("ctx", "head"), None), P(("ctx", "head"), None))
    return jax.shard_map(step, mesh=mesh, in_specs=in_specs, out_specs=out_specs, check_vma=False)
```

```python
import functools
import math

import jax
import jax.numpy as jnp
from jax import lax
from jax.experimental import pallas as pl
from jax.experimental.pallas import tpu as pltpu
from jax.sharding import PartitionSpec as P


HEAD_DIM = 128
BLOCK = 128
REACH = 8


def from_behind(x, axis, by):
    devices = lax.axis_size(axis)
    pairs = [(i, i + by) for i in range(devices) if 0 <= i + by < devices]
    return lax.ppermute(x, axis, pairs)


def requests_of(lists_pad, owner, blocks_here):
    rows = lax.dynamic_slice_in_dim(lists_pad, owner + 1, REACH, 0)
    mine = rows // blocks_here == owner
    return jnp.max(jnp.where(mine, rows % blocks_here, -1), axis=1)


def fetch_tree(kv_local, lists_pad, myself):
    blocks_here = kv_local.shape[0]
    kv_prev = from_behind(kv_local, "ctx", 1)
    req_me = jnp.clip(requests_of(lists_pad, myself, blocks_here), 0, blocks_here - 1)
    req_prev = jnp.clip(requests_of(lists_pad, myself - 1, blocks_here), 0, blocks_here - 1)
    out_me = jnp.take(kv_local, req_me, axis=0)
    out_prev = jnp.take(kv_prev, req_prev[jnp.array([0, 2, 4, 6])], axis=0)
    step2 = from_behind(jnp.stack([out_me[1], out_prev[1], out_me[5], out_prev[3]]), "ctx", 2)
    step4 = from_behind(jnp.stack([out_me[3], out_prev[2], step2[2], step2[3]]), "ctx", 4)
    step8 = from_behind(out_me[7], "ctx", 8)
    return jnp.stack([out_prev[0], step2[0], step2[1], step4[0], step4[1], step4[2], step4[3], step8])


def return_tree(first, rest):
    step4 = from_behind(first, "ctx", -4)
    step8 = from_behind(rest[3], "ctx", -8)
    step2 = from_behind(jnp.stack([rest[1], rest[2], step4[2], step4[3]]), "ctx", -2)
    step1 = from_behind(jnp.stack([rest[0], step2[1], step4[1], step2[3]]), "ctx", -1)
    return jnp.stack([step1[0], step2[0], step1[1], step4[0], step1[2], step2[2], step1[3], step8])


def attn_kernel(slot_ref, use_ref, early_ref, q_ref, g_ref, kv_ref, dq_ref, home_ref, first_ref, rest_ref, kv_scr,
                qs_scr, gs_scr,
                acc_ref, *, chosen, group, scaling):
    n = pl.program_id(0)
    homes = home_ref.shape[0]

    @pl.when(n == 0)
    def _():
        acc_ref[...] = jnp.zeros_like(acc_ref)

    keys = chosen * BLOCK
    for e in range(chosen):
        kv_scr[e * BLOCK:(e + 1) * BLOCK, :] = kv_ref[slot_ref[n * chosen + e]]
    key_cat = kv_scr[:, :HEAD_DIM]
    value_cat = kv_scr[:, HEAD_DIM:]
    for h in range(group):
        qs_scr[h * BLOCK:(h + 1) * BLOCK, :] = q_ref[:, h * HEAD_DIM:(h + 1) * HEAD_DIM]
        gs_scr[h * BLOCK:(h + 1) * BLOCK, :] = g_ref[:, h * HEAD_DIM:(h + 1) * HEAD_DIM]
    q_all = qs_scr[...]
    g_all = gs_scr[...]

    col = lax.broadcasted_iota(jnp.int32, (BLOCK, keys), 1)
    row = lax.broadcasted_iota(jnp.int32, (BLOCK, keys), 0)
    ent = col // BLOCK
    tok = col % BLOCK
    use_col = jnp.zeros((BLOCK, keys), jnp.int32)
    early_col = jnp.zeros((BLOCK, keys), jnp.int32)
    for e in range(chosen):
        use_col = jnp.where(ent == e, use_ref[n * chosen + e], use_col)
        early_col = jnp.where(ent == e, early_ref[n * chosen + e], early_col)
    allowed = (use_col != 0) & ((early_col != 0) | (tok <= row))

    nt = (((1,), (1,)), ((), ()))
    tn = (((0,), (0,)), ((), ()))
    rows = group * BLOCK
    scores = lax.dot_general(q_all, key_cat, nt, preferred_element_type=jnp.float32) * scaling
    scores = scores.reshape(group, BLOCK, keys)
    scores = jnp.where(allowed[None], scores, -1e30)
    row_max = jnp.max(scores, axis=2, keepdims=True)
    total = jnp.sum(jnp.exp(scores - row_max), axis=2, keepdims=True)
    log_total = row_max + jnp.log(total)
    prob = jnp.exp(scores - log_total).reshape(rows, keys)
    prob_half = prob.astype(jnp.bfloat16)
    output = jnp.dot(prob_half, value_cat, preferred_element_type=jnp.float32)
    output = output.astype(jnp.bfloat16).astype(jnp.float32)
    row_dot = jnp.sum(g_all.astype(jnp.float32) * output, axis=1, keepdims=True)
    prob_grad = lax.dot_general(g_all, value_cat, nt, preferred_element_type=jnp.float32)
    score_grad = (prob * (prob_grad - row_dot) * scaling).astype(jnp.bfloat16)
    dq_all = jnp.dot(score_grad, key_cat, preferred_element_type=jnp.float32).astype(jnp.bfloat16)
    for h in range(group):
        dq_ref[:, h * HEAD_DIM:(h + 1) * HEAD_DIM] = dq_all[h * BLOCK:(h + 1) * BLOCK, :]
    key_t = lax.dot_general(q_all, score_grad, tn, preferred_element_type=jnp.float32)
    value_t = lax.dot_general(g_all, prob_half, tn, preferred_element_type=jnp.float32)
    key_part = key_t.T
    value_part = value_t.T

    for e in range(chosen):
        s = slot_ref[n * chosen + e]
        part = slice(e * BLOCK, (e + 1) * BLOCK)
        acc_ref[s, :, :HEAD_DIM] += key_part[part, :]
        acc_ref[s, :, HEAD_DIM:] += value_part[part, :]

    @pl.when(n == pl.num_programs(0) - 1)
    def _():
        home_ref[...] = acc_ref[:homes]
        first_ref[...] = acc_ref[homes + 3:homes + 7].astype(jnp.bfloat16)
        rest_ref[0:3] = acc_ref[homes:homes + 3].astype(jnp.bfloat16)
        rest_ref[3] = acc_ref[homes + 7].astype(jnp.bfloat16)


def attention_terms(slots, usable, earlier, query_states, out_grad, kv_stock, chosen):
    tok_rows, q_cols = query_states.shape
    slot_count = kv_stock.shape[0]
    group = q_cols // HEAD_DIM
    blocks_here = tok_rows // BLOCK
    kernel = functools.partial(attn_kernel, chosen=chosen, group=group, scaling=1.0 / math.sqrt(HEAD_DIM))
    grid_spec = pltpu.PrefetchScalarGridSpec(
        num_scalar_prefetch=3,
        grid=(blocks_here,),
        in_specs=[
            pl.BlockSpec((BLOCK, q_cols), lambda n, *_: (n, 0)),
            pl.BlockSpec((BLOCK, q_cols), lambda n, *_: (n, 0)),
            pl.BlockSpec((slot_count, BLOCK, 2 * HEAD_DIM), lambda n, *_: (0, 0, 0)),
        ],
        out_specs=[
            pl.BlockSpec((BLOCK, q_cols), lambda n, *_: (n, 0)),
            pl.BlockSpec((blocks_here, BLOCK, 2 * HEAD_DIM), lambda n, *_: (0, 0, 0)),
            pl.BlockSpec((4, BLOCK, 2 * HEAD_DIM), lambda n, *_: (0, 0, 0)),
            pl.BlockSpec((4, BLOCK, 2 * HEAD_DIM), lambda n, *_: (0, 0, 0)),
        ],
        scratch_shapes=[
            pltpu.VMEM((chosen * BLOCK, 2 * HEAD_DIM), jnp.bfloat16),
            pltpu.VMEM((group * BLOCK, HEAD_DIM), jnp.bfloat16),
            pltpu.VMEM((group * BLOCK, HEAD_DIM), jnp.bfloat16),
            pltpu.VMEM((slot_count, BLOCK, 2 * HEAD_DIM), jnp.float32),
        ],
    )
    return pl.pallas_call(
        kernel,
        grid_spec=grid_spec,
        out_shape=[
            jax.ShapeDtypeStruct((tok_rows, q_cols), jnp.bfloat16),
            jax.ShapeDtypeStruct((blocks_here, BLOCK, 2 * HEAD_DIM), jnp.float32),
            jax.ShapeDtypeStruct((4, BLOCK, 2 * HEAD_DIM), jnp.bfloat16),
            jax.ShapeDtypeStruct((4, BLOCK, 2 * HEAD_DIM), jnp.bfloat16),
        ],
        compiler_params=pltpu.CompilerParams(dimension_semantics=("arbitrary",)),
    )(slots, usable, earlier, query_states, out_grad, kv_stock)


def step(query_states, key_states, value_states, out_grad, block_lists):
    ctx_count = lax.axis_size("ctx")
    head_count = lax.axis_size("head")
    myself = lax.axis_index("ctx")
    tok_rows = query_states.shape[0]
    kv_cols = key_states.shape[1]
    blocks_here = tok_rows // BLOCK
    chosen = block_lists.shape[1]
    lists_by_dev = block_lists.reshape(ctx_count, blocks_here * chosen)
    slot_ids = jnp.arange(blocks_here, dtype=jnp.int32)
    no_rows = jnp.full((REACH, blocks_here * chosen), -blocks_here, jnp.int32)
    lists_pad = jnp.concatenate([lists_by_dev, no_rows], axis=0)
    kv_local = jnp.concatenate([key_states, value_states], axis=1).reshape(blocks_here, BLOCK, 2 * kv_cols)
    kv_stock = jnp.concatenate([kv_local, fetch_tree(kv_local, lists_pad, myself)], axis=0)
    requested = requests_of(lists_pad, myself, blocks_here)

    own_entries = lax.dynamic_slice_in_dim(block_lists, myself * blocks_here, blocks_here, 0)
    block_ids = myself * blocks_here + slot_ids
    order_ids = jnp.arange(chosen, dtype=jnp.int32)
    repeat = (own_entries[:, :, None] == own_entries[:, None, :]) & (
        order_ids[None, None, :] < order_ids[None, :, None]
    )
    usable = jnp.logical_not(jnp.any(repeat, axis=2))
    earlier = own_entries < block_ids[:, None]
    behind = myself - own_entries // blocks_here
    slots = jnp.where(behind == 0, own_entries % blocks_here, blocks_here - 1 + behind)
    slots = jnp.clip(slots, 0, blocks_here + REACH - 1)

    query_local, home, first, rest = attention_terms(
        slots.reshape(-1).astype(jnp.int32),
        usable.reshape(-1).astype(jnp.int32),
        earlier.reshape(-1).astype(jnp.int32),
        query_states,
        out_grad,
        kv_stock,
        chosen,
    )
    query_grad = lax.all_to_all(query_local, "head", split_axis=0, concat_axis=1, tiled=True)
    arrived = return_tree(first, rest).astype(jnp.float32)
    credit = (requested[None, :] == slot_ids[:, None]).astype(jnp.float32)
    totals = home + jnp.sum(credit[:, :, None, None] * arrived[None], axis=1)
    kv_grad = totals.reshape(tok_rows, 2 * kv_cols).astype(jnp.bfloat16)
    kv_all = lax.all_to_all(kv_grad, "head", split_axis=0, concat_axis=1, tiled=True)
    out_rows = tok_rows // head_count
    kv_all = kv_all.reshape(out_rows, head_count, 2, kv_cols)
    key_grad = kv_all[:, :, 0, :].reshape(out_rows, head_count * kv_cols)
    value_grad = kv_all[:, :, 1, :].reshape(out_rows, head_count * kv_cols)
    return (query_grad, key_grad, value_grad)


def solution(mesh):
    in_specs = (P("ctx", "head"), P("ctx", "head"), P("ctx", "head"), P("ctx", "head"), P())
    out_specs = (P(("ctx", "head"), None), P(("ctx", "head"), None), P(("ctx", "head"), None))
    return jax.shard_map(step, mesh=mesh, in_specs=in_specs, out_specs=out_specs, check_vma=False)
```

```python
import functools
import math

import jax
import jax.numpy as jnp
from jax import lax
from jax.experimental import pallas as pl
from jax.experimental.pallas import tpu as pltpu
from jax.sharding import PartitionSpec as P


HEAD_DIM = 128
BLOCK = 128
REACH = 8


def from_behind(x, axis, by):
    devices = lax.axis_size(axis)
    pairs = [(i, i + by) for i in range(devices) if 0 <= i + by < devices]
    return lax.ppermute(x, axis, pairs)


def requests_of(lists_pad, owner, blocks_here):
    rows = lax.dynamic_slice_in_dim(lists_pad, owner + 1, REACH, 0)
    mine = rows // blocks_here == owner
    return jnp.max(jnp.where(mine, rows % blocks_here, -1), axis=1)


def fetch_tree(kv_local, lists_pad, myself):
    blocks_here = kv_local.shape[0]
    kv_prev = from_behind(kv_local, "ctx", 1)
    req_me = jnp.clip(requests_of(lists_pad, myself, blocks_here), 0, blocks_here - 1)
    req_prev = jnp.clip(requests_of(lists_pad, myself - 1, blocks_here), 0, blocks_here - 1)
    out_me = jnp.take(kv_local, req_me, axis=0)
    out_prev = jnp.take(kv_prev, req_prev[jnp.array([0, 2, 4, 6])], axis=0)
    step2 = from_behind(jnp.stack([out_me[1], out_prev[1], out_me[5], out_prev[3]]), "ctx", 2)
    step4 = from_behind(jnp.stack([out_me[3], out_prev[2], step2[2], step2[3]]), "ctx", 4)
    step8 = from_behind(out_me[7], "ctx", 8)
    return jnp.stack([out_prev[0], step2[0], step2[1], step4[0], step4[1], step4[2], step4[3], step8])


def return_tree(first, rest):
    step4 = from_behind(first, "ctx", -4)
    step8 = from_behind(rest[3], "ctx", -8)
    step2 = from_behind(jnp.stack([rest[1], rest[2], step4[2], step4[3]]), "ctx", -2)
    step1 = from_behind(jnp.stack([rest[0], step2[1], step4[1], step2[3]]), "ctx", -1)
    return jnp.stack([step1[0], step2[0], step1[1], step4[0], step1[2], step2[2], step1[3], step8])


def attn_kernel(slot_ref, use_ref, early_ref, q_ref, g_ref, near_ref, far_ref, dq_ref, home_ref, first_ref, rest_ref, kv_scr,
                qs_scr, gs_scr,
                acc_ref, *, chosen, group, scaling):
    n = pl.program_id(0)
    homes = home_ref.shape[0]

    @pl.when(n == 0)
    def _():
        acc_ref[...] = jnp.zeros_like(acc_ref)

    keys = chosen * BLOCK
    near = near_ref.shape[0]
    for e in range(chosen):
        slot = slot_ref[n * chosen + e]
        rows_e = slice(e * BLOCK, (e + 1) * BLOCK)

        @pl.when(slot < near)
        def _():
            kv_scr[rows_e, :] = near_ref[jnp.minimum(slot, near - 1)]

        @pl.when(slot >= near)
        def _():
            kv_scr[rows_e, :] = far_ref[jnp.maximum(slot - near, 0)]
    key_cat = kv_scr[:, :HEAD_DIM]
    value_cat = kv_scr[:, HEAD_DIM:]
    for h in range(group):
        qs_scr[h * BLOCK:(h + 1) * BLOCK, :] = q_ref[:, h * HEAD_DIM:(h + 1) * HEAD_DIM]
        gs_scr[h * BLOCK:(h + 1) * BLOCK, :] = g_ref[:, h * HEAD_DIM:(h + 1) * HEAD_DIM]
    q_all = qs_scr[...]
    g_all = gs_scr[...]

    col = lax.broadcasted_iota(jnp.int32, (1, keys), 1)
    ent = col // BLOCK
    use_col = jnp.zeros((1, keys), jnp.int32)
    early_col = jnp.zeros((1, keys), jnp.int32)
    for e in range(chosen):
        use_col = jnp.where(ent == e, use_ref[n * chosen + e], use_col)
        early_col = jnp.where(ent == e, early_ref[n * chosen + e], early_col)
    first_row = jnp.where(use_col != 0, jnp.where(early_col != 0, 0, col % BLOCK), BLOCK)
    row = lax.broadcasted_iota(jnp.int32, (BLOCK, keys), 0)
    allowed = row >= first_row

    nt = (((1,), (1,)), ((), ()))
    tn = (((0,), (0,)), ((), ()))
    rows = group * BLOCK
    scores = lax.dot_general(q_all, key_cat, nt, preferred_element_type=jnp.float32) * scaling
    scores = scores.reshape(group, BLOCK, keys)
    scores = jnp.where(allowed[None], scores, -1e30)
    row_max = jnp.max(scores, axis=2, keepdims=True)
    total = jnp.sum(jnp.exp(scores - row_max), axis=2, keepdims=True)
    log_total = row_max + jnp.log(total)
    prob = jnp.exp(scores - log_total).reshape(rows, keys)
    prob_half = prob.astype(jnp.bfloat16)
    output = jnp.dot(prob_half, value_cat, preferred_element_type=jnp.float32)
    output = output.astype(jnp.bfloat16).astype(jnp.float32)
    row_dot = jnp.sum(g_all.astype(jnp.float32) * output, axis=1, keepdims=True)
    prob_grad = lax.dot_general(g_all, value_cat, nt, preferred_element_type=jnp.float32)
    score_grad = (prob * (prob_grad - row_dot) * scaling).astype(jnp.bfloat16)
    dq_all = jnp.dot(score_grad, key_cat, preferred_element_type=jnp.float32).astype(jnp.bfloat16)
    for h in range(group):
        dq_ref[:, h * HEAD_DIM:(h + 1) * HEAD_DIM] = dq_all[h * BLOCK:(h + 1) * BLOCK, :]
    key_t = lax.dot_general(q_all, score_grad, tn, preferred_element_type=jnp.float32)
    value_t = lax.dot_general(g_all, prob_half, tn, preferred_element_type=jnp.float32)
    key_part = key_t.T
    value_part = value_t.T

    for e in range(chosen):
        s = slot_ref[n * chosen + e]
        part = slice(e * BLOCK, (e + 1) * BLOCK)
        acc_ref[s, :, :HEAD_DIM] += key_part[part, :]
        acc_ref[s, :, HEAD_DIM:] += value_part[part, :]

    @pl.when(n == pl.num_programs(0) - 1)
    def _():
        home_ref[...] = acc_ref[:homes]
        first_ref[...] = acc_ref[homes + 3:homes + 7].astype(jnp.bfloat16)
        rest_ref[0:3] = acc_ref[homes:homes + 3].astype(jnp.bfloat16)
        rest_ref[3] = acc_ref[homes + 7].astype(jnp.bfloat16)


def attention_terms(slots, usable, earlier, query_states, out_grad, kv_near, kv_far, chosen):
    tok_rows, q_cols = query_states.shape
    slot_count = kv_near.shape[0] + kv_far.shape[0]
    group = q_cols // HEAD_DIM
    blocks_here = tok_rows // BLOCK
    kernel = functools.partial(attn_kernel, chosen=chosen, group=group, scaling=1.0 / math.sqrt(HEAD_DIM))
    grid_spec = pltpu.PrefetchScalarGridSpec(
        num_scalar_prefetch=3,
        grid=(blocks_here,),
        in_specs=[
            pl.BlockSpec((BLOCK, q_cols), lambda n, *_: (n, 0)),
            pl.BlockSpec((BLOCK, q_cols), lambda n, *_: (n, 0)),
            pl.BlockSpec(kv_near.shape, lambda n, *_: (0, 0, 0)),
            pl.BlockSpec(kv_far.shape, lambda n, *_: (0, 0, 0)),
        ],
        out_specs=[
            pl.BlockSpec((BLOCK, q_cols), lambda n, *_: (n, 0)),
            pl.BlockSpec((blocks_here, BLOCK, 2 * HEAD_DIM), lambda n, *_: (0, 0, 0)),
            pl.BlockSpec((4, BLOCK, 2 * HEAD_DIM), lambda n, *_: (0, 0, 0)),
            pl.BlockSpec((4, BLOCK, 2 * HEAD_DIM), lambda n, *_: (0, 0, 0)),
        ],
        scratch_shapes=[
            pltpu.VMEM((chosen * BLOCK, 2 * HEAD_DIM), jnp.bfloat16),
            pltpu.VMEM((group * BLOCK, HEAD_DIM), jnp.bfloat16),
            pltpu.VMEM((group * BLOCK, HEAD_DIM), jnp.bfloat16),
            pltpu.VMEM((slot_count, BLOCK, 2 * HEAD_DIM), jnp.float32),
        ],
    )
    return pl.pallas_call(
        kernel,
        grid_spec=grid_spec,
        out_shape=[
            jax.ShapeDtypeStruct((tok_rows, q_cols), jnp.bfloat16),
            jax.ShapeDtypeStruct((blocks_here, BLOCK, 2 * HEAD_DIM), jnp.float32),
            jax.ShapeDtypeStruct((4, BLOCK, 2 * HEAD_DIM), jnp.bfloat16),
            jax.ShapeDtypeStruct((4, BLOCK, 2 * HEAD_DIM), jnp.bfloat16),
        ],
        compiler_params=pltpu.CompilerParams(dimension_semantics=("arbitrary",)),
    )(slots, usable, earlier, query_states, out_grad, kv_near, kv_far)


def step(query_states, key_states, value_states, out_grad, block_lists):
    ctx_count = lax.axis_size("ctx")
    head_count = lax.axis_size("head")
    myself = lax.axis_index("ctx")
    tok_rows = query_states.shape[0]
    kv_cols = key_states.shape[1]
    blocks_here = tok_rows // BLOCK
    chosen = block_lists.shape[1]
    lists_by_dev = block_lists.reshape(ctx_count, blocks_here * chosen)
    slot_ids = jnp.arange(blocks_here, dtype=jnp.int32)
    no_rows = jnp.full((REACH, blocks_here * chosen), -blocks_here, jnp.int32)
    lists_pad = jnp.concatenate([lists_by_dev, no_rows], axis=0)
    kv_local = jnp.concatenate([key_states, value_states], axis=1).reshape(blocks_here, BLOCK, 2 * kv_cols)
    kv_far = fetch_tree(kv_local, lists_pad, myself)
    requested = requests_of(lists_pad, myself, blocks_here)

    own_entries = lax.dynamic_slice_in_dim(block_lists, myself * blocks_here, blocks_here, 0)
    block_ids = myself * blocks_here + slot_ids
    order_ids = jnp.arange(chosen, dtype=jnp.int32)
    repeat = (own_entries[:, :, None] == own_entries[:, None, :]) & (
        order_ids[None, None, :] < order_ids[None, :, None]
    )
    usable = jnp.logical_not(jnp.any(repeat, axis=2))
    earlier = own_entries < block_ids[:, None]
    behind = myself - own_entries // blocks_here
    slots = jnp.where(behind == 0, own_entries % blocks_here, blocks_here - 1 + behind)
    slots = jnp.clip(slots, 0, blocks_here + REACH - 1)

    query_local, home, first, rest = attention_terms(
        slots.reshape(-1).astype(jnp.int32),
        usable.reshape(-1).astype(jnp.int32),
        earlier.reshape(-1).astype(jnp.int32),
        query_states,
        out_grad,
        kv_local,
        kv_far,
        chosen,
    )
    query_grad = lax.all_to_all(query_local, "head", split_axis=0, concat_axis=1, tiled=True)
    arrived = return_tree(first, rest).astype(jnp.float32)
    credit = (requested[None, :] == slot_ids[:, None]).astype(jnp.float32)
    totals = home + jnp.sum(credit[:, :, None, None] * arrived[None], axis=1)
    kv_grad = totals.reshape(tok_rows, 2 * kv_cols).astype(jnp.bfloat16)
    kv_all = lax.all_to_all(kv_grad, "head", split_axis=0, concat_axis=1, tiled=True)
    out_rows = tok_rows // head_count
    kv_all = kv_all.reshape(out_rows, head_count, 2, kv_cols)
    key_grad = kv_all[:, :, 0, :].reshape(out_rows, head_count * kv_cols)
    value_grad = kv_all[:, :, 1, :].reshape(out_rows, head_count * kv_cols)
    return (query_grad, key_grad, value_grad)


def solution(mesh):
    in_specs = (P("ctx", "head"), P("ctx", "head"), P("ctx", "head"), P("ctx", "head"), P())
    out_specs = (P(("ctx", "head"), None), P(("ctx", "head"), None), P(("ctx", "head"), None))
    return jax.shard_map(step, mesh=mesh, in_specs=in_specs, out_specs=out_specs, check_vma=False)
```

```python
import functools
import math

import jax
import jax.numpy as jnp
from jax import lax
from jax.experimental import pallas as pl
from jax.experimental.pallas import tpu as pltpu
from jax.sharding import PartitionSpec as P


HEAD_DIM = 128
BLOCK = 128
REACH = 8


def from_behind(x, axis, by):
    devices = lax.axis_size(axis)
    pairs = [(i, i + by) for i in range(devices) if 0 <= i + by < devices]
    return lax.ppermute(x, axis, pairs)


def requests_of(lists_pad, owner, blocks_here):
    rows = lax.dynamic_slice_in_dim(lists_pad, owner + 1, REACH, 0)
    mine = rows // blocks_here == owner
    return jnp.max(jnp.where(mine, rows % blocks_here, -1), axis=1)


def fetch_tree(kv_local, lists_pad, myself):
    blocks_here = kv_local.shape[0]
    kv_prev = from_behind(kv_local, "ctx", 1)
    req_me = jnp.clip(requests_of(lists_pad, myself, blocks_here), 0, blocks_here - 1)
    req_prev = jnp.clip(requests_of(lists_pad, myself - 1, blocks_here), 0, blocks_here - 1)
    out_me = jnp.take(kv_local, req_me, axis=0)
    out_prev = jnp.take(kv_prev, req_prev[jnp.array([0, 2, 4, 6])], axis=0)
    step2 = from_behind(jnp.stack([out_me[1], out_prev[1], out_me[5], out_prev[3]]), "ctx", 2)
    step4 = from_behind(jnp.stack([out_me[3], out_prev[2], step2[2], step2[3]]), "ctx", 4)
    step8 = from_behind(out_me[7], "ctx", 8)
    return jnp.stack([out_prev[0], step2[0], step2[1], step4[0], step4[1], step4[2], step4[3], step8])


def return_tree(first, rest):
    step4 = from_behind(first, "ctx", -4)
    step8 = from_behind(rest[3], "ctx", -8)
    step2 = from_behind(jnp.stack([rest[1], rest[2], step4[2], step4[3]]), "ctx", -2)
    step1 = from_behind(jnp.stack([rest[0], step2[1], step4[1], step2[3]]), "ctx", -1)
    return jnp.stack([step1[0], step2[0], step1[1], step4[0], step1[2], step2[2], step1[3], step8])


def attn_kernel(slot_ref, use_ref, early_ref, q_ref, g_ref, near_ref, far_ref, dq_ref, home_ref, first_ref, rest_ref, kv_scr,
                qs_scr, gs_scr,
                acc_ref, *, chosen, group, scaling):
    n = pl.program_id(0)
    homes = home_ref.shape[0]

    @pl.when(n == 0)
    def _():
        acc_ref[...] = jnp.zeros_like(acc_ref)

    keys = chosen * BLOCK
    near = near_ref.shape[0]
    for e in range(chosen):
        slot = slot_ref[n * chosen + e]
        rows_e = slice(e * BLOCK, (e + 1) * BLOCK)

        @pl.when(slot < near)
        def _():
            kv_scr[rows_e, :] = near_ref[jnp.minimum(slot, near - 1)]

        @pl.when(slot >= near)
        def _():
            kv_scr[rows_e, :] = far_ref[jnp.maximum(slot - near, 0)]
    key_cat = kv_scr[:, :HEAD_DIM]
    value_cat = kv_scr[:, HEAD_DIM:]
    for h in range(group):
        qs_scr[h * BLOCK:(h + 1) * BLOCK, :] = q_ref[:, h * HEAD_DIM:(h + 1) * HEAD_DIM]
        gs_scr[h * BLOCK:(h + 1) * BLOCK, :] = g_ref[:, h * HEAD_DIM:(h + 1) * HEAD_DIM]
    q_all = qs_scr[...]
    g_all = gs_scr[...]

    col = lax.broadcasted_iota(jnp.int32, (1, keys), 1)
    ent = col // BLOCK
    use_col = jnp.zeros((1, keys), jnp.int32)
    early_col = jnp.zeros((1, keys), jnp.int32)
    for e in range(chosen):
        use_col = jnp.where(ent == e, use_ref[n * chosen + e], use_col)
        early_col = jnp.where(ent == e, early_ref[n * chosen + e], early_col)
    first_row = jnp.where(use_col != 0, jnp.where(early_col != 0, 0, col % BLOCK), BLOCK)
    row = lax.broadcasted_iota(jnp.int32, (BLOCK, keys), 0)
    allowed = row >= first_row

    nt = (((1,), (1,)), ((), ()))
    tn = (((0,), (0,)), ((), ()))
    rows = group * BLOCK
    scores = lax.dot_general(q_all, key_cat, nt, preferred_element_type=jnp.float32) * scaling
    scores = scores.reshape(group, BLOCK, keys)
    scores = jnp.where(allowed[None], scores, -1e30)
    row_max = jnp.max(scores, axis=2, keepdims=True)
    total = jnp.sum(jnp.exp(scores - row_max), axis=2, keepdims=True)
    log_total = row_max + jnp.log(total)
    prob = jnp.exp(scores - log_total).reshape(rows, keys)
    prob_half = prob.astype(jnp.bfloat16)
    output = jnp.dot(prob_half, value_cat, preferred_element_type=jnp.float32)
    output = output.astype(jnp.bfloat16).astype(jnp.float32)
    row_dot = jnp.sum(g_all.astype(jnp.float32) * output, axis=1, keepdims=True)
    prob_grad = lax.dot_general(g_all, value_cat, nt, preferred_element_type=jnp.float32)
    score_grad = (prob * (prob_grad - row_dot) * scaling).astype(jnp.bfloat16)
    dq_all = jnp.dot(score_grad, key_cat, preferred_element_type=jnp.float32).astype(jnp.bfloat16)
    for h in range(group):
        dq_ref[:, h * HEAD_DIM:(h + 1) * HEAD_DIM] = dq_all[h * BLOCK:(h + 1) * BLOCK, :]
    key_t = lax.dot_general(q_all, score_grad, tn, preferred_element_type=jnp.float32)
    value_t = lax.dot_general(g_all, prob_half, tn, preferred_element_type=jnp.float32)
    key_part = key_t.T
    value_part = value_t.T

    for e in range(chosen):
        s = slot_ref[n * chosen + e]
        part = slice(e * BLOCK, (e + 1) * BLOCK)
        acc_ref[s, :, :HEAD_DIM] += key_part[part, :]
        acc_ref[s, :, HEAD_DIM:] += value_part[part, :]

    @pl.when(n == pl.num_programs(0) - 1)
    def _():
        home_ref[...] = acc_ref[:homes]
        first_ref[...] = acc_ref[homes + 3:homes + 7].astype(jnp.bfloat16)
        rest_ref[0:3] = acc_ref[homes:homes + 3].astype(jnp.bfloat16)
        rest_ref[3] = acc_ref[homes + 7].astype(jnp.bfloat16)


def attention_terms(slots, usable, earlier, query_states, out_grad, kv_near, kv_far, chosen):
    tok_rows, q_cols = query_states.shape
    slot_count = kv_near.shape[0] + kv_far.shape[0]
    group = q_cols // HEAD_DIM
    blocks_here = tok_rows // BLOCK
    kernel = functools.partial(attn_kernel, chosen=chosen, group=group, scaling=1.0 / math.sqrt(HEAD_DIM))
    grid_spec = pltpu.PrefetchScalarGridSpec(
        num_scalar_prefetch=3,
        grid=(blocks_here,),
        in_specs=[
            pl.BlockSpec((BLOCK, q_cols), lambda n, *_: (n, 0)),
            pl.BlockSpec((BLOCK, q_cols), lambda n, *_: (n, 0)),
            pl.BlockSpec(kv_near.shape, lambda n, *_: (0, 0, 0)),
            pl.BlockSpec(kv_far.shape, lambda n, *_: (0, 0, 0)),
        ],
        out_specs=[
            pl.BlockSpec((BLOCK, q_cols), lambda n, *_: (n, 0)),
            pl.BlockSpec((blocks_here, BLOCK, 2 * HEAD_DIM), lambda n, *_: (0, 0, 0)),
            pl.BlockSpec((4, BLOCK, 2 * HEAD_DIM), lambda n, *_: (0, 0, 0)),
            pl.BlockSpec((4, BLOCK, 2 * HEAD_DIM), lambda n, *_: (0, 0, 0)),
        ],
        scratch_shapes=[
            pltpu.VMEM((chosen * BLOCK, 2 * HEAD_DIM), jnp.bfloat16),
            pltpu.VMEM((group * BLOCK, HEAD_DIM), jnp.bfloat16),
            pltpu.VMEM((group * BLOCK, HEAD_DIM), jnp.bfloat16),
            pltpu.VMEM((slot_count, BLOCK, 2 * HEAD_DIM), jnp.float32),
        ],
    )
    return pl.pallas_call(
        kernel,
        grid_spec=grid_spec,
        out_shape=[
            jax.ShapeDtypeStruct((tok_rows, q_cols), jnp.bfloat16),
            jax.ShapeDtypeStruct((blocks_here, BLOCK, 2 * HEAD_DIM), jnp.float32),
            jax.ShapeDtypeStruct((4, BLOCK, 2 * HEAD_DIM), jnp.bfloat16),
            jax.ShapeDtypeStruct((4, BLOCK, 2 * HEAD_DIM), jnp.bfloat16),
        ],
        compiler_params=pltpu.CompilerParams(dimension_semantics=("arbitrary",)),
    )(slots, usable, earlier, query_states, out_grad, kv_near, kv_far)


def step(query_states, key_states, value_states, out_grad, block_lists):
    ctx_count = lax.axis_size("ctx")
    head_count = lax.axis_size("head")
    myself = lax.axis_index("ctx")
    tok_rows = query_states.shape[0]
    kv_cols = key_states.shape[1]
    blocks_here = tok_rows // BLOCK
    chosen = block_lists.shape[1]
    lists_by_dev = block_lists.reshape(ctx_count, blocks_here * chosen)
    slot_ids = jnp.arange(blocks_here, dtype=jnp.int32)
    no_rows = jnp.full((REACH, blocks_here * chosen), -blocks_here, jnp.int32)
    lists_pad = jnp.concatenate([lists_by_dev, no_rows], axis=0)
    kv_local = jnp.concatenate([key_states, value_states], axis=1).reshape(blocks_here, BLOCK, 2 * kv_cols)
    kv_far = fetch_tree(kv_local, lists_pad, myself)
    requested = requests_of(lists_pad, myself, blocks_here)

    own_entries = lax.dynamic_slice_in_dim(block_lists, myself * blocks_here, blocks_here, 0)
    block_ids = myself * blocks_here + slot_ids
    order_ids = jnp.arange(chosen, dtype=jnp.int32)
    repeat = (own_entries[:, :, None] == own_entries[:, None, :]) & (
        order_ids[None, None, :] < order_ids[None, :, None]
    )
    usable = jnp.logical_not(jnp.any(repeat, axis=2))
    earlier = own_entries < block_ids[:, None]
    behind = myself - own_entries // blocks_here
    slots = jnp.where(behind == 0, own_entries % blocks_here, blocks_here - 1 + behind)
    slots = jnp.clip(slots, 0, blocks_here + REACH - 1)

    query_local, home, first, rest = attention_terms(
        slots.reshape(-1).astype(jnp.int32),
        usable.reshape(-1).astype(jnp.int32),
        earlier.reshape(-1).astype(jnp.int32),
        query_states,
        out_grad,
        kv_local,
        kv_far,
        chosen,
    )
    query_grad = lax.all_to_all(query_local, "head", split_axis=0, concat_axis=1, tiled=True)
    arrived = return_tree(first, rest)
    totals = home
    for d in range(REACH):
        credit = (requested[d] == slot_ids)[:, None, None]
        totals = totals + jnp.where(credit, arrived[d][None].astype(jnp.float32), 0.0)
    kv_grad = totals.reshape(tok_rows, 2 * kv_cols).astype(jnp.bfloat16)
    kv_all = lax.all_to_all(kv_grad, "head", split_axis=0, concat_axis=1, tiled=True)
    out_rows = tok_rows // head_count
    kv_all = kv_all.reshape(out_rows, head_count, 2, kv_cols)
    key_grad = kv_all[:, :, 0, :].reshape(out_rows, head_count * kv_cols)
    value_grad = kv_all[:, :, 1, :].reshape(out_rows, head_count * kv_cols)
    return (query_grad, key_grad, value_grad)


def solution(mesh):
    in_specs = (P("ctx", "head"), P("ctx", "head"), P("ctx", "head"), P("ctx", "head"), P())
    out_specs = (P(("ctx", "head"), None), P(("ctx", "head"), None), P(("ctx", "head"), None))
    return jax.shard_map(step, mesh=mesh, in_specs=in_specs, out_specs=out_specs, check_vma=False)
```
